1024 devices in a mesh: ctx: 128 (over y, z), head: 8 (over x, core).
Axes of the slice: x: 4, y: 4, z: 32, core: 2. Of those that a mesh axis runs over, the one named last changes fastest.
Arguments:
- query_rows: bfloat16 [16384, 2048], P('ctx', 'head'), may hold values from -40 to 40
- key_rows: bfloat16 [16384, 2048], P('ctx', 'head'), may hold values from -6 to 6
- value_rows: bfloat16 [16384, 2048], P('ctx', 'head'), may hold values from -40 to 40
- norm_gain: bfloat16 [2048], P('head'), may hold values from 0.099609375 to 1.8984375
- cotangent: bfloat16 [16384, 2048], P('ctx', 'head'), may hold values from -6 to 6
Outputs:
- normed: bfloat16 [16384, 2048], P('ctx', 'head')
- query_grad: bfloat16 [16384, 2048], P('ctx', 'head')
- key_grad: bfloat16 [16384, 2048], P('ctx', 'head')
- value_grad: bfloat16 [16384, 2048], P('ctx', 'head')
The draws below stay inside these ranges and needn't reach their ends.
All inputs are finite; a program needn't handle non-finite values.
Results may differ from the reference program's by a relative error of at most 0.0058.
Values sent between devices are 32-bit elements; how exact they have to be, the bound alone decides.
No kernel may reach another device: no remote copies, remote signals or barrier semaphores. Data moves between devices by JAX's collectives and lax.ppermute only.
A program may use at most 64 MiB of HBM per device.

```python
import jax
import jax.numpy as jnp
from jax import lax

HEADS = 32
HEAD_DIM = 64
TOK_DEV = 128
TOKENS = 16384
WIDTH = 2048
N_CTX = 128


def draw_query_rows(key, part):
    first, second = jax.random.split(jax.random.fold_in(key, 11))
    base = jnp.clip(jax.random.normal(first, (TOKENS, HEADS * HEAD_DIM), jnp.float32), -4.0, 4.0)
    scale = 10.0 ** jax.random.uniform(second, (TOKENS, 1), jnp.float32, 0.0, 1.0)
    return (base * scale).astype(jnp.bfloat16)


def draw_value_rows(key, part):
    first, second = jax.random.split(jax.random.fold_in(key, 23))
    head_index = jnp.arange(HEADS * HEAD_DIM) // HEAD_DIM
    jitter = jax.random.uniform(second, (HEADS,), jnp.float32, 0.0, 1.0)
    ramp = head_index.astype(jnp.float32) / (HEADS - 1)
    base = jnp.clip(jax.random.normal(first, (TOKENS, HEADS * HEAD_DIM), jnp.float32), -4.0, 4.0)
    scale = 10.0 ** (0.5 * ramp + 0.5 * jitter[head_index])
    return (base * scale[None, :]).astype(jnp.bfloat16)


def levels(key, extent, pieces, least, top_value):
    loudness = 1.0
    for position, parts in pieces:
        steps = jax.random.uniform(jax.random.fold_in(jax.random.fold_in(key, 6), position), (parts,), jnp.float32, least / len(pieces), top_value / len(pieces))
        loudness = loudness * jnp.repeat(jnp.exp(steps), extent[position] // parts).reshape((-1,) + (1,) * (len(extent) - 1 - position))
    return loudness


def scatter_about(key, extent, deviation, bound, cuts=(), held_as=jnp.bfloat16):
    values = deviation * jax.random.normal(key, extent, jnp.float32)
    if cuts:
        values = values * levels(key, extent, cuts, -0.22, 0.18)
    return jnp.clip(values, -bound, bound).astype(held_as)


def setup_inputs(seed: int = 0) -> dict:
    arg_keys = jax.random.split(jax.random.key(seed), 6)
    query_rows = draw_query_rows(jax.random.fold_in(arg_keys[5], 71), 0)
    key_rows = scatter_about(arg_keys[1], (TOKENS, WIDTH), 1.0, 6.0, ((0, 128), (1, 8)))
    value_rows = draw_value_rows(jax.random.fold_in(arg_keys[5], 71), 0)
    norm_gain = jnp.clip(1.0 + 0.18 * jax.random.normal(arg_keys[3], (WIDTH,), jnp.float32), 0.099609375, 1.8984375).astype(jnp.bfloat16)
    cotangent = scatter_about(arg_keys[4], (TOKENS, WIDTH), 1.0, 6.0, ((0, 128), (1, 8)))
    return dict(query_rows=query_rows, key_rows=key_rows, value_rows=value_rows, norm_gain=norm_gain, cotangent=cotangent)


EPS = 1e-05

def reference(query_rows, key_rows, value_rows, norm_gain, cotangent):
    width_all = HEADS * HEAD_DIM

    def blocks(array):
        return array.reshape(N_CTX, TOK_DEV, HEADS, HEAD_DIM)
    gain = norm_gain.astype(jnp.float32)
    causal = jnp.tril(jnp.ones((TOK_DEV, TOK_DEV), dtype=bool))

    def forward(state, inputs):
        query, keyblk, value, upper = inputs
        qf = query.astype(jnp.float32)
        kf = keyblk.astype(jnp.float32)
        vf = value.astype(jnp.float32)
        scores = jnp.einsum('thd,shd->hts', qf, kf)
        masked = jnp.where(causal[None], scores, 0.0).astype(jnp.bfloat16)
        carried = state.astype(jnp.bfloat16)
        output = jnp.einsum('hts,shd->thd', masked.astype(jnp.float32), vf)
        output = output + jnp.einsum('thd,hde->the', qf, carried.astype(jnp.float32))
        flat = output.reshape(TOK_DEV, width_all)
        recip = lax.rsqrt(lax.optimization_barrier(jnp.mean(flat * flat, axis=1)) + EPS)
        result = (flat * recip[:, None] * gain).astype(jnp.bfloat16)
        upstream = upper.reshape(TOK_DEV, width_all).astype(jnp.float32) * gain
        inner = lax.optimization_barrier(jnp.sum(upstream * flat, axis=1))
        grad_flat = recip[:, None] * upstream - flat * (recip * recip * recip * inner / width_all)[:, None]
        grad_out = grad_flat.astype(jnp.bfloat16).reshape(TOK_DEV, HEADS, HEAD_DIM)
        gof = grad_out.astype(jnp.float32)
        grad_scores = jnp.where(causal[None], jnp.einsum('thd,shd->hts', gof, vf), 0.0).astype(jnp.bfloat16)
        grad_query = jnp.einsum('hts,shd->thd', grad_scores.astype(jnp.float32), kf)
        grad_query = grad_query + jnp.einsum('the,hde->thd', gof, carried.astype(jnp.float32))
        new_state = state + jnp.einsum('thd,the->hde', kf, vf)
        return (new_state, (result, grad_query.astype(jnp.bfloat16), grad_out))
    start = jnp.zeros((HEADS, HEAD_DIM, HEAD_DIM), jnp.float32)
    inputs = (blocks(query_rows), blocks(key_rows), blocks(value_rows), blocks(cotangent))
    unused, (results, query_grads, grad_outs) = lax.scan(forward, start, inputs)

    def backward(state, inputs):
        query, keyblk, value, grad_out = inputs
        qf = query.astype(jnp.float32)
        kf = keyblk.astype(jnp.float32)
        vf = value.astype(jnp.float32)
        gof = grad_out.astype(jnp.float32)
        masked = jnp.where(causal[None], jnp.einsum('thd,shd->hts', qf, kf), 0.0).astype(jnp.bfloat16)
        grad_scores = jnp.where(causal[None], jnp.einsum('thd,shd->hts', gof, vf), 0.0).astype(jnp.bfloat16)
        later = state.astype(jnp.bfloat16).astype(jnp.float32)
        grad_key = jnp.einsum('hts,thd->shd', grad_scores.astype(jnp.float32), qf)
        grad_key = grad_key + jnp.einsum('she,hde->shd', vf, later)
        grad_value = jnp.einsum('hts,thd->shd', masked.astype(jnp.float32), gof)
        grad_value = grad_value + jnp.einsum('shd,hde->she', kf, later)
        new_state = state + jnp.einsum('thd,the->hde', qf, gof)
        return (new_state, (grad_key.astype(jnp.bfloat16), grad_value.astype(jnp.bfloat16)))
    back_inputs = (blocks(query_rows), blocks(key_rows), blocks(value_rows), grad_outs)
    unused_back, (key_grads, value_grads) = lax.scan(backward, start, back_inputs, reverse=True)
    shape = (N_CTX * TOK_DEV, width_all)
    return (results.reshape(shape), query_grads.reshape(shape), key_grads.reshape(shape), value_grads.reshape(shape))
```

```python
import jax
import jax.numpy as jnp
from jax import lax
from jax.sharding import PartitionSpec as P

HEADS = 32
HEAD_DIM = 64


EPS = 1e-05


def prefix(value, axis, reverse):
    peers = lax.axis_size(axis)
    rows = value.reshape(peers, -1)
    mine = lax.all_to_all(rows, axis, 0, 0, tiled=True)
    if reverse:
        mine = mine[::-1]
    shifted = jnp.concatenate([jnp.zeros_like(mine[:1]), mine[:-1]], axis=0)
    total = jnp.cumsum(shifted, axis=0)
    if reverse:
        total = total[::-1]
    back = lax.all_to_all(total, axis, 0, 0, tiled=True)
    return lax.optimization_barrier(back).reshape(value.shape)


def on_device(query_rows, key_rows, value_rows, norm_gain, cotangent):
    tokens_here = query_rows.shape[0]
    heads_here = query_rows.shape[1] // HEAD_DIM
    width_all = HEADS * HEAD_DIM

    def split_heads(array):
        return array.reshape(tokens_here, heads_here, HEAD_DIM)

    queries = split_heads(query_rows)
    key_local = split_heads(key_rows)
    value_local = split_heads(value_rows)
    gain = norm_gain.astype(jnp.float32)
    causal = lax.broadcasted_iota(jnp.int32, (tokens_here, tokens_here), 0) >= lax.broadcasted_iota(
        jnp.int32, (tokens_here, tokens_here), 1
    )
    local_state = jnp.einsum(
        "thd,the->hde", key_local, value_local, preferred_element_type=jnp.float32
    )
    carried = prefix(local_state, "ctx", False)
    carried_bf = carried.astype(jnp.bfloat16)
    scores = jnp.einsum("thd,shd->hts", queries, key_local, preferred_element_type=jnp.float32)
    masked = jnp.where(causal[None], scores, 0.0).astype(jnp.bfloat16)
    attended = jnp.einsum("hts,shd->thd", masked, value_local, preferred_element_type=jnp.float32)
    attended = attended + jnp.einsum(
        "thd,hde->the", queries, carried_bf, preferred_element_type=jnp.float32
    )
    flat = attended.reshape(tokens_here, heads_here * HEAD_DIM)
    square_local = jnp.sum(flat * flat, axis=1)
    upstream = cotangent.astype(jnp.float32) * gain
    inner_local = jnp.sum(upstream * flat, axis=1)
    square_all = lax.psum(square_local, "head")
    recip = lax.rsqrt(square_all / width_all + EPS)
    normed = (flat * recip[:, None] * gain).astype(jnp.bfloat16)
    inner_all = lax.psum(inner_local, "head")
    grad_flat = (
        recip[:, None] * upstream - flat * (recip * recip * recip * inner_all / width_all)[:, None]
    )
    grad_out = split_heads(grad_flat.astype(jnp.bfloat16))
    grad_scores = jnp.einsum(
        "thd,shd->hts", grad_out, value_local, preferred_element_type=jnp.float32
    )
    grad_masked = jnp.where(causal[None], grad_scores, 0.0).astype(jnp.bfloat16)
    query_grad = jnp.einsum(
        "hts,shd->thd", grad_masked, key_local, preferred_element_type=jnp.float32
    )
    query_grad = query_grad + jnp.einsum(
        "the,hde->thd", grad_out, carried_bf, preferred_element_type=jnp.float32
    )
    local_grad = jnp.einsum("thd,the->hde", queries, grad_out, preferred_element_type=jnp.float32)
    later = prefix(local_grad, "ctx", True)
    later_bf = later.astype(jnp.bfloat16)
    key_grad = jnp.einsum("hts,thd->shd", grad_masked, queries, preferred_element_type=jnp.float32)
    key_grad = key_grad + jnp.einsum(
        "she,hde->shd", value_local, later_bf, preferred_element_type=jnp.float32
    )
    value_grad = jnp.einsum("hts,thd->shd", masked, grad_out, preferred_element_type=jnp.float32)
    value_grad = value_grad + jnp.einsum(
        "shd,hde->she", key_local, later_bf, preferred_element_type=jnp.float32
    )
    shape = (tokens_here, heads_here * HEAD_DIM)
    return (
        normed,
        query_grad.reshape(shape).astype(jnp.bfloat16),
        key_grad.reshape(shape).astype(jnp.bfloat16),
        value_grad.reshape(shape).astype(jnp.bfloat16),
    )


def solution(mesh):
    placed = (P("ctx", "head"), P("ctx", "head"), P("ctx", "head"), P("head"), P("ctx", "head"))
    return jax.shard_map(
        on_device,
        mesh=mesh,
        in_specs=placed,
        out_specs=(P("ctx", "head"), P("ctx", "head"), P("ctx", "head"), P("ctx", "head")),
        check_vma=False,
    )
```

```python
import jax
import jax.numpy as jnp
from jax import lax
from jax.sharding import PartitionSpec as P

HEADS = 32
HEAD_DIM = 64


EPS = 1e-05


def prefix(value, axis, reverse):
    peers = lax.axis_size(axis)
    rows = value.reshape(peers, -1)
    mine = lax.all_to_all(rows, axis, 0, 0, tiled=True)
    total = lax.cumsum(mine, axis=0, reverse=reverse)
    zero = jnp.zeros_like(total[:1])
    if reverse:
        total = jnp.concatenate([total[1:], zero], axis=0)
    else:
        total = jnp.concatenate([zero, total[:-1]], axis=0)
    back = lax.all_to_all(total, axis, 0, 0, tiled=True)
    return lax.optimization_barrier(back).reshape(value.shape)


def head_sum(value, axis):
    peers = lax.axis_size(axis)
    spread = jnp.broadcast_to(value[None], (peers,) + value.shape)
    gathered = lax.all_to_all(spread, axis, 0, 0, tiled=True)
    return jnp.sum(gathered, axis=0)


def on_device(query_rows, key_rows, value_rows, norm_gain, cotangent):
    tokens_here = query_rows.shape[0]
    heads_here = query_rows.shape[1] // HEAD_DIM
    width_all = HEADS * HEAD_DIM

    def split_heads(array):
        return array.reshape(tokens_here, heads_here, HEAD_DIM)

    queries = split_heads(query_rows)
    key_local = split_heads(key_rows)
    value_local = split_heads(value_rows)
    gain = norm_gain.astype(jnp.float32)
    causal = lax.broadcasted_iota(jnp.int32, (tokens_here, tokens_here), 0) >= lax.broadcasted_iota(
        jnp.int32, (tokens_here, tokens_here), 1
    )
    local_state = jnp.einsum(
        "thd,the->hde", key_local, value_local, preferred_element_type=jnp.float32
    )
    carried = prefix(local_state, "ctx", False)
    carried_bf = carried.astype(jnp.bfloat16)
    scores = jnp.einsum("thd,shd->hts", queries, key_local, preferred_element_type=jnp.float32)
    masked = jnp.where(causal[None], scores, 0.0).astype(jnp.bfloat16)
    attended = jnp.einsum("hts,shd->thd", masked, value_local, preferred_element_type=jnp.float32)
    attended = attended + jnp.einsum(
        "thd,hde->the", queries, carried_bf, preferred_element_type=jnp.float32
    )
    flat = attended.reshape(tokens_here, heads_here * HEAD_DIM)
    square_local = jnp.sum(flat * flat, axis=1)
    upstream = cotangent.astype(jnp.float32) * gain
    inner_local = jnp.sum(upstream * flat, axis=1)
    square_all, inner_all = head_sum(jnp.stack([square_local, inner_local]), "head")
    recip = lax.rsqrt(square_all / width_all + EPS)
    normed = (flat * recip[:, None] * gain).astype(jnp.bfloat16)
    grad_flat = (
        recip[:, None] * upstream - flat * (recip * recip * recip * inner_all / width_all)[:, None]
    )
    grad_out = split_heads(grad_flat.astype(jnp.bfloat16))
    grad_scores = jnp.einsum(
        "thd,shd->hts", grad_out, value_local, preferred_element_type=jnp.float32
    )
    grad_masked = jnp.where(causal[None], grad_scores, 0.0).astype(jnp.bfloat16)
    query_grad = jnp.einsum(
        "hts,shd->thd", grad_masked, key_local, preferred_element_type=jnp.float32
    )
    query_grad = query_grad + jnp.einsum(
        "the,hde->thd", grad_out, carried_bf, preferred_element_type=jnp.float32
    )
    local_grad = jnp.einsum("thd,the->hde", queries, grad_out, preferred_element_type=jnp.float32)
    later = prefix(local_grad, "ctx", True)
    later_bf = later.astype(jnp.bfloat16)
    key_grad = jnp.einsum("hts,thd->shd", grad_masked, queries, preferred_element_type=jnp.float32)
    key_grad = key_grad + jnp.einsum(
        "she,hde->shd", value_local, later_bf, preferred_element_type=jnp.float32
    )
    value_grad = jnp.einsum("hts,thd->shd", masked, grad_out, preferred_element_type=jnp.float32)
    value_grad = value_grad + jnp.einsum(
        "shd,hde->she", key_local, later_bf, preferred_element_type=jnp.float32
    )
    shape = (tokens_here, heads_here * HEAD_DIM)
    return (
        normed,
        query_grad.reshape(shape).astype(jnp.bfloat16),
        key_grad.reshape(shape).astype(jnp.bfloat16),
        value_grad.reshape(shape).astype(jnp.bfloat16),
    )


def solution(mesh):
    placed = (P("ctx", "head"), P("ctx", "head"), P("ctx", "head"), P("head"), P("ctx", "head"))
    return jax.shard_map(
        on_device,
        mesh=mesh,
        in_specs=placed,
        out_specs=(P("ctx", "head"), P("ctx", "head"), P("ctx", "head"), P("ctx", "head")),
        check_vma=False,
    )
```

```python
import jax
import jax.numpy as jnp
from jax import lax
from jax.sharding import PartitionSpec as P

HEADS = 32
HEAD_DIM = 64


EPS = 1e-05


def prefix(value, axis, reverse):
    peers = lax.axis_size(axis)
    rows = value.reshape(peers, -1)
    mine = lax.all_to_all(rows, axis, 0, 0, tiled=True)
    row = lax.broadcasted_iota(jnp.int32, (peers, peers), 0)
    col = lax.broadcasted_iota(jnp.int32, (peers, peers), 1)
    before = (col > row) if reverse else (col < row)
    total = jnp.dot(before.astype(mine.dtype), mine, precision=lax.Precision.HIGHEST)
    back = lax.all_to_all(total, axis, 0, 0, tiled=True)
    return lax.optimization_barrier(back).reshape(value.shape)


def head_sum(value, axis):
    peers = lax.axis_size(axis)
    spread = jnp.broadcast_to(value[None], (peers,) + value.shape)
    gathered = lax.all_to_all(spread, axis, 0, 0, tiled=True)
    return jnp.sum(gathered, axis=0)


def on_device(query_rows, key_rows, value_rows, norm_gain, cotangent):
    tokens_here = query_rows.shape[0]
    heads_here = query_rows.shape[1] // HEAD_DIM
    width_all = HEADS * HEAD_DIM

    def split_heads(array):
        return array.reshape(tokens_here, heads_here, HEAD_DIM)

    queries = split_heads(query_rows)
    key_local = split_heads(key_rows)
    value_local = split_heads(value_rows)
    gain = norm_gain.astype(jnp.float32)
    causal = lax.broadcasted_iota(jnp.int32, (tokens_here, tokens_here), 0) >= lax.broadcasted_iota(
        jnp.int32, (tokens_here, tokens_here), 1
    )
    local_state = jnp.einsum(
        "thd,the->hde", key_local, value_local, preferred_element_type=jnp.float32
    )
    carried = prefix(local_state, "ctx", False)
    carried_bf = carried.astype(jnp.bfloat16)
    scores = jnp.einsum("thd,shd->hts", queries, key_local, preferred_element_type=jnp.float32)
    masked = jnp.where(causal[None], scores, 0.0).astype(jnp.bfloat16)
    attended = jnp.einsum("hts,shd->thd", masked, value_local, preferred_element_type=jnp.float32)
    attended = attended + jnp.einsum(
        "thd,hde->the", queries, carried_bf, preferred_element_type=jnp.float32
    )
    flat = attended.reshape(tokens_here, heads_here * HEAD_DIM)
    square_local = jnp.sum(flat * flat, axis=1)
    upstream = cotangent.astype(jnp.float32) * gain
    inner_local = jnp.sum(upstream * flat, axis=1)
    square_all, inner_all = head_sum(jnp.stack([square_local, inner_local]), "head")
    recip = lax.rsqrt(square_all / width_all + EPS)
    normed = (flat * recip[:, None] * gain).astype(jnp.bfloat16)
    grad_flat = (
        recip[:, None] * upstream - flat * (recip * recip * recip * inner_all / width_all)[:, None]
    )
    grad_out = split_heads(grad_flat.astype(jnp.bfloat16))
    grad_scores = jnp.einsum(
        "thd,shd->hts", grad_out, value_local, preferred_element_type=jnp.float32
    )
    grad_masked = jnp.where(causal[None], grad_scores, 0.0).astype(jnp.bfloat16)
    query_grad = jnp.einsum(
        "hts,shd->thd", grad_masked, key_local, preferred_element_type=jnp.float32
    )
    query_grad = query_grad + jnp.einsum(
        "the,hde->thd", grad_out, carried_bf, preferred_element_type=jnp.float32
    )
    local_grad = jnp.einsum("thd,the->hde", queries, grad_out, preferred_element_type=jnp.float32)
    later = prefix(local_grad, "ctx", True)
    later_bf = later.astype(jnp.bfloat16)
    key_grad = jnp.einsum("hts,thd->shd", grad_masked, queries, preferred_element_type=jnp.float32)
    key_grad = key_grad + jnp.einsum(
        "she,hde->shd", value_local, later_bf, preferred_element_type=jnp.float32
    )
    value_grad = jnp.einsum("hts,thd->shd", masked, grad_out, preferred_element_type=jnp.float32)
    value_grad = value_grad + jnp.einsum(
        "shd,hde->she", key_local, later_bf, preferred_element_type=jnp.float32
    )
    shape = (tokens_here, heads_here * HEAD_DIM)
    return (
        normed,
        query_grad.reshape(shape).astype(jnp.bfloat16),
        key_grad.reshape(shape).astype(jnp.bfloat16),
        value_grad.reshape(shape).astype(jnp.bfloat16),
    )


def solution(mesh):
    placed = (P("ctx", "head"), P("ctx", "head"), P("ctx", "head"), P("head"), P("ctx", "head"))
    return jax.shard_map(
        on_device,
        mesh=mesh,
        in_specs=placed,
        out_specs=(P("ctx", "head"), P("ctx", "head"), P("ctx", "head"), P("ctx", "head")),
        check_vma=False,
    )
```

```python
import jax
import jax.numpy as jnp
from jax import lax
from jax.sharding import PartitionSpec as P

HEADS = 32
HEAD_DIM = 64


EPS = 1e-05


def prefix(value, axis, reverse):
    peers = lax.axis_size(axis)
    rows = value.reshape(peers, -1)
    mine = lax.all_to_all(rows, axis, 0, 0, tiled=True)
    row = lax.broadcasted_iota(jnp.int32, (peers, peers), 0)
    col = lax.broadcasted_iota(jnp.int32, (peers, peers), 1)
    before = (col > row) if reverse else (col < row)
    total = jnp.dot(before.astype(mine.dtype), mine, precision=lax.Precision.HIGHEST)
    back = lax.all_to_all(total, axis, 0, 0, tiled=True)
    return lax.optimization_barrier(back).reshape(value.shape)


def head_sum(value, axis):
    peers = lax.axis_size(axis)
    spread = jnp.broadcast_to(value[None], (peers,) + value.shape)
    gathered = lax.all_to_all(spread, axis, 0, 0, tiled=True)
    return jnp.sum(gathered, axis=0)


def on_device(query_rows, key_rows, value_rows, norm_gain, cotangent):
    tokens_here = query_rows.shape[0]
    heads_here = query_rows.shape[1] // HEAD_DIM
    width_all = HEADS * HEAD_DIM

    def split_heads(array):
        return array.reshape(tokens_here, heads_here, HEAD_DIM)

    queries = split_heads(query_rows)
    key_local = split_heads(key_rows)
    value_local = split_heads(value_rows)
    gain = norm_gain.astype(jnp.float32)
    causal = lax.broadcasted_iota(jnp.int32, (tokens_here, tokens_here), 0) >= lax.broadcasted_iota(
        jnp.int32, (tokens_here, tokens_here), 1
    )
    every_pair = lax.dot_general(
        key_rows, value_rows, (((0,), (0,)), ((), ())), preferred_element_type=jnp.float32
    )
    local_state = jnp.stack(
        [every_pair[h * HEAD_DIM:(h + 1) * HEAD_DIM, h * HEAD_DIM:(h + 1) * HEAD_DIM] for h in range(heads_here)]
    )
    carried = prefix(local_state, "ctx", False)
    carried_bf = carried.astype(jnp.bfloat16)
    scores = jnp.einsum("thd,shd->hts", queries, key_local, preferred_element_type=jnp.float32)
    masked = jnp.where(causal[None], scores, 0.0).astype(jnp.bfloat16)
    attended = jnp.einsum("hts,shd->thd", masked, value_local, preferred_element_type=jnp.float32)
    attended = attended + jnp.einsum(
        "thd,hde->the", queries, carried_bf, preferred_element_type=jnp.float32
    )
    flat = attended.reshape(tokens_here, heads_here * HEAD_DIM)
    square_local = jnp.sum(flat * flat, axis=1)
    upstream = cotangent.astype(jnp.float32) * gain
    inner_local = jnp.sum(upstream * flat, axis=1)
    square_all, inner_all = head_sum(jnp.stack([square_local, inner_local]), "head")
    recip = lax.rsqrt(square_all / width_all + EPS)
    normed = (flat * recip[:, None] * gain).astype(jnp.bfloat16)
    grad_flat = (
        recip[:, None] * upstream - flat * (recip * recip * recip * inner_all / width_all)[:, None]
    )
    grad_out = split_heads(grad_flat.astype(jnp.bfloat16))
    grad_scores = jnp.einsum(
        "thd,shd->hts", grad_out, value_local, preferred_element_type=jnp.float32
    )
    grad_masked = jnp.where(causal[None], grad_scores, 0.0).astype(jnp.bfloat16)
    query_grad = jnp.einsum(
        "hts,shd->thd", grad_masked, key_local, preferred_element_type=jnp.float32
    )
    query_grad = query_grad + jnp.einsum(
        "the,hde->thd", grad_out, carried_bf, preferred_element_type=jnp.float32
    )
    local_grad = jnp.einsum("thd,the->hde", queries, grad_out, preferred_element_type=jnp.float32)
    later = prefix(local_grad, "ctx", True)
    later_bf = later.astype(jnp.bfloat16)
    width_here = heads_here * HEAD_DIM
    same_head = (
        lax.broadcasted_iota(jnp.int32, (width_here, width_here), 0) // HEAD_DIM
        == lax.broadcasted_iota(jnp.int32, (width_here, width_here), 1) // HEAD_DIM
    )
    tiled = jnp.tile(later_bf.reshape(width_here, HEAD_DIM), (1, heads_here))
    by_value = jnp.where(same_head, tiled, jnp.zeros_like(tiled))
    by_key = jnp.where(same_head, tiled.T, jnp.zeros_like(tiled))
    key_grad = jnp.einsum("hts,thd->shd", grad_masked, queries, preferred_element_type=jnp.float32)
    key_grad = key_grad.reshape(tokens_here, width_here) + jnp.dot(
        value_rows, by_key, preferred_element_type=jnp.float32
    )
    value_grad = jnp.einsum("hts,thd->shd", masked, grad_out, preferred_element_type=jnp.float32)
    value_grad = value_grad.reshape(tokens_here, width_here) + jnp.dot(
        key_rows, by_value, preferred_element_type=jnp.float32
    )
    shape = (tokens_here, heads_here * HEAD_DIM)
    return (
        normed,
        query_grad.reshape(shape).astype(jnp.bfloat16),
        key_grad.reshape(shape).astype(jnp.bfloat16),
        value_grad.reshape(shape).astype(jnp.bfloat16),
    )


def solution(mesh):
    placed = (P("ctx", "head"), P("ctx", "head"), P("ctx", "head"), P("head"), P("ctx", "head"))
    return jax.shard_map(
        on_device,
        mesh=mesh,
        in_specs=placed,
        out_specs=(P("ctx", "head"), P("ctx", "head"), P("ctx", "head"), P("ctx", "head")),
        check_vma=False,
    )
```

```python
import jax
import jax.numpy as jnp
from jax import lax
from jax.sharding import Mesh, PartitionSpec as P

HEADS = 32
HEAD_DIM = 64


EPS = 1e-05


def prefix(value, axes, reverse):
    rows_axis, cols_axis = axes
    rows_n, cols_n = lax.axis_size(rows_axis), lax.axis_size(cols_axis)
    peers = rows_n * cols_n
    rows = value.reshape(peers, -1)
    mine = lax.all_to_all(rows, (cols_axis, rows_axis), 0, 0, tiled=True)
    slot = lax.broadcasted_iota(jnp.int32, (peers,), 0)
    order = (slot % rows_n) * cols_n + slot // rows_n
    row, col = order[:, None], order[None, :]
    before = (col > row) if reverse else (col < row)
    total = jnp.dot(before.astype(mine.dtype), mine, precision=lax.Precision.HIGHEST)
    back = lax.all_to_all(total, (cols_axis, rows_axis), 0, 0, tiled=True)
    return lax.optimization_barrier(back).reshape(value.shape)


def head_sum(value, axis):
    peers = lax.axis_size(axis)
    spread = jnp.broadcast_to(value[None], (peers,) + value.shape)
    gathered = lax.all_to_all(spread, axis, 0, 0, tiled=True)
    return jnp.sum(gathered, axis=0)


def on_device(query_rows, key_rows, value_rows, norm_gain, cotangent):
    tokens_here = query_rows.shape[0]
    heads_here = query_rows.shape[1] // HEAD_DIM
    width_all = HEADS * HEAD_DIM

    def split_heads(array):
        return array.reshape(tokens_here, heads_here, HEAD_DIM)

    queries = split_heads(query_rows)
    key_local = split_heads(key_rows)
    value_local = split_heads(value_rows)
    gain = norm_gain.astype(jnp.float32)
    causal = lax.broadcasted_iota(jnp.int32, (tokens_here, tokens_here), 0) >= lax.broadcasted_iota(
        jnp.int32, (tokens_here, tokens_here), 1
    )
    local_state = jnp.einsum(
        "thd,the->hde", key_local, value_local, preferred_element_type=jnp.float32
    )
    carried = prefix(local_state, ("ctx_rows", "ctx_cols"), False)
    carried_bf = carried.astype(jnp.bfloat16)
    scores = jnp.einsum("thd,shd->hts", queries, key_local, preferred_element_type=jnp.float32)
    masked = jnp.where(causal[None], scores, 0.0).astype(jnp.bfloat16)
    attended = jnp.einsum("hts,shd->thd", masked, value_local, preferred_element_type=jnp.float32)
    attended = attended + jnp.einsum(
        "thd,hde->the", queries, carried_bf, preferred_element_type=jnp.float32
    )
    flat = attended.reshape(tokens_here, heads_here * HEAD_DIM)
    square_local = jnp.sum(flat * flat, axis=1)
    upstream = cotangent.astype(jnp.float32) * gain
    inner_local = jnp.sum(upstream * flat, axis=1)
    square_all, inner_all = head_sum(jnp.stack([square_local, inner_local]), "head")
    recip = lax.rsqrt(square_all / width_all + EPS)
    normed = (flat * recip[:, None] * gain).astype(jnp.bfloat16)
    grad_flat = (
        recip[:, None] * upstream - flat * (recip * recip * recip * inner_all / width_all)[:, None]
    )
    grad_out = split_heads(grad_flat.astype(jnp.bfloat16))
    grad_scores = jnp.einsum(
        "thd,shd->hts", grad_out, value_local, preferred_element_type=jnp.float32
    )
    grad_masked = jnp.where(causal[None], grad_scores, 0.0).astype(jnp.bfloat16)
    query_grad = jnp.einsum(
        "hts,shd->thd", grad_masked, key_local, preferred_element_type=jnp.float32
    )
    query_grad = query_grad + jnp.einsum(
        "the,hde->thd", grad_out, carried_bf, preferred_element_type=jnp.float32
    )
    local_grad = jnp.einsum("thd,the->hde", queries, grad_out, preferred_element_type=jnp.float32)
    later = prefix(local_grad, ("ctx_rows", "ctx_cols"), True)
    later_bf = later.astype(jnp.bfloat16)
    key_grad = jnp.einsum("hts,thd->shd", grad_masked, queries, preferred_element_type=jnp.float32)
    key_grad = key_grad + jnp.einsum(
        "she,hde->shd", value_local, later_bf, preferred_element_type=jnp.float32
    )
    value_grad = jnp.einsum("hts,thd->shd", masked, grad_out, preferred_element_type=jnp.float32)
    value_grad = value_grad + jnp.einsum(
        "shd,hde->she", key_local, later_bf, preferred_element_type=jnp.float32
    )
    shape = (tokens_here, heads_here * HEAD_DIM)
    return (
        normed,
        query_grad.reshape(shape).astype(jnp.bfloat16),
        key_grad.reshape(shape).astype(jnp.bfloat16),
        value_grad.reshape(shape).astype(jnp.bfloat16),
    )


def ctx_split(mesh):
    ctx_devices = mesh.devices[:, 0]
    rows_n = len({device.coords[1] for device in ctx_devices})
    return rows_n, len(ctx_devices) // rows_n


def solution(mesh):
    rows_n, cols_n = ctx_split(mesh)
    heads_n = mesh.devices.shape[1]
    split = Mesh(mesh.devices.reshape(rows_n, cols_n, heads_n), ("ctx_rows", "ctx_cols", "head"))
    rows = P(("ctx_rows", "ctx_cols"), "head")
    placed = (rows, rows, rows, P("head"), rows)
    return jax.shard_map(
        on_device,
        mesh=split,
        in_specs=placed,
        out_specs=(rows, rows, rows, rows),
        check_vma=False,
    )
```

```python
import jax
import jax.numpy as jnp
from jax import lax
from jax.sharding import Mesh, PartitionSpec as P

HEADS = 32
HEAD_DIM = 64


EPS = 1e-05


def prefix(value, axes, reverse):
    rows_axis, cols_axis = axes
    rows_n, cols_n = lax.axis_size(rows_axis), lax.axis_size(cols_axis)
    peers = rows_n * cols_n
    rows = value.reshape(peers, -1)
    mine = lax.all_to_all(rows, (cols_axis, rows_axis), 0, 0, tiled=True)
    slot = lax.broadcasted_iota(jnp.int32, (peers,), 0)
    order = (slot % rows_n) * cols_n + slot // rows_n
    row, col = order[:, None], order[None, :]
    before = (col > row) if reverse else (col < row)
    total = jnp.dot(before.astype(mine.dtype), mine, precision=lax.Precision.HIGHEST)
    back = lax.all_to_all(total, (cols_axis, rows_axis), 0, 0, tiled=True)
    return lax.optimization_barrier(back).reshape(value.shape)


def head_sum(value, axis):
    peers = lax.axis_size(axis)
    spread = jnp.broadcast_to(value[None], (peers,) + value.shape)
    gathered = lax.all_to_all(spread, axis, 0, 0, tiled=True)
    return jnp.sum(gathered, axis=0)


def on_device(query_rows, key_rows, value_rows, norm_gain, cotangent):
    tokens_here = query_rows.shape[0]
    heads_here = query_rows.shape[1] // HEAD_DIM
    width_all = HEADS * HEAD_DIM

    def split_heads(array):
        return array.reshape(tokens_here, heads_here, HEAD_DIM)

    queries = split_heads(query_rows)
    key_local = split_heads(key_rows)
    value_local = split_heads(value_rows)
    gain = norm_gain.astype(jnp.float32)
    causal = lax.broadcasted_iota(jnp.int32, (tokens_here, tokens_here), 0) >= lax.broadcasted_iota(
        jnp.int32, (tokens_here, tokens_here), 1
    )
    local_state = jnp.einsum(
        "thd,the->hde", key_local, value_local, preferred_element_type=jnp.float32
    )
    carried = prefix(local_state, ("ctx_rows", "ctx_cols"), False)
    carried_bf = carried.astype(jnp.bfloat16)
    scores = jnp.einsum("thd,shd->hts", queries, key_local, preferred_element_type=jnp.float32)
    masked = jnp.where(causal[None], scores, 0.0).astype(jnp.bfloat16)
    attended = jnp.einsum("hts,shd->thd", masked, value_local, preferred_element_type=jnp.float32)
    attended = attended + jnp.einsum(
        "thd,hde->the", queries, carried_bf, preferred_element_type=jnp.float32
    )
    flat = attended.reshape(tokens_here, heads_here * HEAD_DIM)
    square_local = jnp.sum(flat * flat, axis=1)
    upstream = cotangent.astype(jnp.float32) * gain
    inner_local = jnp.sum(upstream * flat, axis=1)
    square_all, inner_all = head_sum(jnp.stack([square_local, inner_local]), ("head_cores", "head_chips"))
    recip = lax.rsqrt(square_all / width_all + EPS)
    normed = (flat * recip[:, None] * gain).astype(jnp.bfloat16)
    grad_flat = (
        recip[:, None] * upstream - flat * (recip * recip * recip * inner_all / width_all)[:, None]
    )
    grad_out = split_heads(grad_flat.astype(jnp.bfloat16))
    grad_scores = jnp.einsum(
        "thd,shd->hts", grad_out, value_local, preferred_element_type=jnp.float32
    )
    grad_masked = jnp.where(causal[None], grad_scores, 0.0).astype(jnp.bfloat16)
    query_grad = jnp.einsum(
        "hts,shd->thd", grad_masked, key_local, preferred_element_type=jnp.float32
    )
    query_grad = query_grad + jnp.einsum(
        "the,hde->thd", grad_out, carried_bf, preferred_element_type=jnp.float32
    )
    local_grad = jnp.einsum("thd,the->hde", queries, grad_out, preferred_element_type=jnp.float32)
    later = prefix(local_grad, ("ctx_rows", "ctx_cols"), True)
    later_bf = later.astype(jnp.bfloat16)
    key_grad = jnp.einsum("hts,thd->shd", grad_masked, queries, preferred_element_type=jnp.float32)
    key_grad = key_grad + jnp.einsum(
        "she,hde->shd", value_local, later_bf, preferred_element_type=jnp.float32
    )
    value_grad = jnp.einsum("hts,thd->shd", masked, grad_out, preferred_element_type=jnp.float32)
    value_grad = value_grad + jnp.einsum(
        "shd,hde->she", key_local, later_bf, preferred_element_type=jnp.float32
    )
    shape = (tokens_here, heads_here * HEAD_DIM)
    return (
        normed,
        query_grad.reshape(shape).astype(jnp.bfloat16),
        key_grad.reshape(shape).astype(jnp.bfloat16),
        value_grad.reshape(shape).astype(jnp.bfloat16),
    )


def axis_split(devices, coord):
    first = len({device.coords[coord] for device in devices})
    return first, len(devices) // first


def solution(mesh):
    rows_n, cols_n = axis_split(mesh.devices[:, 0], 1)
    chips_n, cores_n = axis_split(mesh.devices[0, :], 0)
    split = Mesh(
        mesh.devices.reshape(rows_n, cols_n, chips_n, cores_n),
        ("ctx_rows", "ctx_cols", "head_chips", "head_cores"),
    )
    rows = P(("ctx_rows", "ctx_cols"), ("head_chips", "head_cores"))
    placed = (rows, rows, rows, P(("head_chips", "head_cores")), rows)
    return jax.shard_map(
        on_device,
        mesh=split,
        in_specs=placed,
        out_specs=(rows, rows, rows, rows),
        check_vma=False,
    )
```

```python
import jax
import jax.numpy as jnp
from jax import lax
from jax.sharding import Mesh, PartitionSpec as P

HEADS = 32
HEAD_DIM = 64


EPS = 1e-05


CTX_AXES = ("ctx_rows", "ctx_hi", "ctx_lo")
PEER_AXES = ("ctx_lo", "ctx_hi", "ctx_rows")


def ctx_of_peer(peers):
    sizes = {axis: lax.axis_size(axis) for axis in CTX_AXES}
    slot = lax.broadcasted_iota(jnp.int32, (peers,), 0)
    place = {}
    for axis in reversed(PEER_AXES):
        place[axis] = slot % sizes[axis]
        slot = slot // sizes[axis]
    index = jnp.zeros((peers,), jnp.int32)
    for axis in CTX_AXES:
        index = index * sizes[axis] + place[axis]
    return index


def prefix(value, reverse):
    peers = lax.axis_size(CTX_AXES)
    rows = value.reshape(peers, -1)
    mine = lax.all_to_all(rows, PEER_AXES, 0, 0, tiled=True)
    order = ctx_of_peer(peers)
    row, col = order[:, None], order[None, :]
    before = (col > row) if reverse else (col < row)
    total = jnp.dot(before.astype(mine.dtype), mine, precision=lax.Precision.HIGHEST)
    back = lax.all_to_all(total, PEER_AXES, 0, 0, tiled=True)
    return lax.optimization_barrier(back).reshape(value.shape)


def head_sum(value, axis):
    peers = lax.axis_size(axis)
    spread = jnp.broadcast_to(value[None], (peers,) + value.shape)
    gathered = lax.all_to_all(spread, axis, 0, 0, tiled=True)
    return jnp.sum(gathered, axis=0)


def on_device(query_rows, key_rows, value_rows, norm_gain, cotangent):
    tokens_here = query_rows.shape[0]
    heads_here = query_rows.shape[1] // HEAD_DIM
    width_all = HEADS * HEAD_DIM

    def split_heads(array):
        return array.reshape(tokens_here, heads_here, HEAD_DIM)

    queries = split_heads(query_rows)
    key_local = split_heads(key_rows)
    value_local = split_heads(value_rows)
    gain = norm_gain.astype(jnp.float32)
    causal = lax.broadcasted_iota(jnp.int32, (tokens_here, tokens_here), 0) >= lax.broadcasted_iota(
        jnp.int32, (tokens_here, tokens_here), 1
    )
    local_state = jnp.einsum(
        "thd,the->hde", key_local, value_local, preferred_element_type=jnp.float32
    )
    carried = prefix(local_state, False)
    carried_bf = carried.astype(jnp.bfloat16)
    scores = jnp.einsum("thd,shd->hts", queries, key_local, preferred_element_type=jnp.float32)
    masked = jnp.where(causal[None], scores, 0.0).astype(jnp.bfloat16)
    attended = jnp.einsum("hts,shd->thd", masked, value_local, preferred_element_type=jnp.float32)
    attended = attended + jnp.einsum(
        "thd,hde->the", queries, carried_bf, preferred_element_type=jnp.float32
    )
    flat = attended.reshape(tokens_here, heads_here * HEAD_DIM)
    square_local = jnp.sum(flat * flat, axis=1)
    upstream = cotangent.astype(jnp.float32) * gain
    inner_local = jnp.sum(upstream * flat, axis=1)
    square_all, inner_all = head_sum(jnp.stack([square_local, inner_local]), "head")
    recip = lax.rsqrt(square_all / width_all + EPS)
    normed = (flat * recip[:, None] * gain).astype(jnp.bfloat16)
    grad_flat = (
        recip[:, None] * upstream - flat * (recip * recip * recip * inner_all / width_all)[:, None]
    )
    grad_out = split_heads(grad_flat.astype(jnp.bfloat16))
    grad_scores = jnp.einsum(
        "thd,shd->hts", grad_out, value_local, preferred_element_type=jnp.float32
    )
    grad_masked = jnp.where(causal[None], grad_scores, 0.0).astype(jnp.bfloat16)
    query_grad = jnp.einsum(
        "hts,shd->thd", grad_masked, key_local, preferred_element_type=jnp.float32
    )
    query_grad = query_grad + jnp.einsum(
        "the,hde->thd", grad_out, carried_bf, preferred_element_type=jnp.float32
    )
    local_grad = jnp.einsum("thd,the->hde", queries, grad_out, preferred_element_type=jnp.float32)
    later = prefix(local_grad, True)
    later_bf = later.astype(jnp.bfloat16)
    key_grad = jnp.einsum("hts,thd->shd", grad_masked, queries, preferred_element_type=jnp.float32)
    key_grad = key_grad + jnp.einsum(
        "she,hde->shd", value_local, later_bf, preferred_element_type=jnp.float32
    )
    value_grad = jnp.einsum("hts,thd->shd", masked, grad_out, preferred_element_type=jnp.float32)
    value_grad = value_grad + jnp.einsum(
        "shd,hde->she", key_local, later_bf, preferred_element_type=jnp.float32
    )
    shape = (tokens_here, heads_here * HEAD_DIM)
    return (
        normed,
        query_grad.reshape(shape).astype(jnp.bfloat16),
        key_grad.reshape(shape).astype(jnp.bfloat16),
        value_grad.reshape(shape).astype(jnp.bfloat16),
    )


def ctx_split(mesh):
    ctx_devices = mesh.devices[:, 0]
    rows_n = len({device.coords[1] for device in ctx_devices})
    cols_n = len(ctx_devices) // rows_n
    return rows_n, 2, cols_n // 2


def solution(mesh):
    heads_n = mesh.devices.shape[1]
    split = Mesh(mesh.devices.reshape(ctx_split(mesh) + (heads_n,)), CTX_AXES + ("head",))
    rows = P(CTX_AXES, "head")
    placed = (rows, rows, rows, P("head"), rows)
    return jax.shard_map(
        on_device,
        mesh=split,
        in_specs=placed,
        out_specs=(rows, rows, rows, rows),
        check_vma=False,
    )
```

```python
import jax
import jax.numpy as jnp
from jax import lax
from jax.sharding import Mesh, PartitionSpec as P

HEADS = 32
HEAD_DIM = 64


EPS = 1e-05


CTX_AXES = ("ctx_rows", "ctx_hi", "ctx_lo")
PEER_AXES = ("ctx_lo", "ctx_hi", "ctx_rows")


def ctx_of_peer(peers):
    sizes = {axis: lax.axis_size(axis) for axis in CTX_AXES}
    slot = lax.broadcasted_iota(jnp.int32, (peers,), 0)
    place = {}
    for axis in reversed(PEER_AXES):
        place[axis] = slot % sizes[axis]
        slot = slot // sizes[axis]
    index = jnp.zeros((peers,), jnp.int32)
    for axis in CTX_AXES:
        index = index * sizes[axis] + place[axis]
    return index


def prefix(value, reverse):
    peers = lax.axis_size(CTX_AXES)
    rows = value.reshape(peers, -1)
    mine = lax.all_to_all(rows, PEER_AXES, 0, 0, tiled=True)
    order = ctx_of_peer(peers)
    row, col = order[:, None], order[None, :]
    before = (col > row) if reverse else (col < row)
    total = jnp.dot(before.astype(mine.dtype), mine, precision=lax.Precision.HIGHEST)
    back = lax.all_to_all(total, PEER_AXES, 0, 0, tiled=True)
    return lax.optimization_barrier(back).reshape(value.shape)


def head_sum(value, axis):
    peers = lax.axis_size(axis)
    spread = jnp.broadcast_to(value[None], (peers,) + value.shape)
    gathered = lax.all_to_all(spread, axis, 0, 0, tiled=True)
    return jnp.sum(gathered, axis=0)


def on_device(query_rows, key_rows, value_rows, norm_gain, cotangent):
    tokens_here = query_rows.shape[0]
    heads_here = query_rows.shape[1] // HEAD_DIM
    width_all = HEADS * HEAD_DIM

    def split_heads(array):
        return array.reshape(tokens_here, heads_here, HEAD_DIM)

    queries = split_heads(query_rows)
    key_local = split_heads(key_rows)
    value_local = split_heads(value_rows)
    gain = norm_gain.astype(jnp.float32)
    causal = lax.broadcasted_iota(jnp.int32, (tokens_here, tokens_here), 0) >= lax.broadcasted_iota(
        jnp.int32, (tokens_here, tokens_here), 1
    )
    local_state = jnp.einsum(
        "thd,the->hde", key_local, value_local, preferred_element_type=jnp.float32
    )
    carried = prefix(local_state, False)
    carried_bf = carried.astype(jnp.bfloat16)
    scores = jnp.einsum("thd,shd->hts", queries, key_local, preferred_element_type=jnp.float32)
    masked = jnp.where(causal[None], scores, 0.0).astype(jnp.bfloat16)
    attended = jnp.einsum("hts,shd->thd", masked, value_local, preferred_element_type=jnp.float32)
    attended = attended + jnp.einsum(
        "thd,hde->the", queries, carried_bf, preferred_element_type=jnp.float32
    )
    flat = attended.reshape(tokens_here, heads_here * HEAD_DIM)
    square_local = jnp.sum(flat * flat, axis=1)
    upstream = cotangent.astype(jnp.float32) * gain
    inner_local = jnp.sum(upstream * flat, axis=1)
    square_all, inner_all = head_sum(jnp.stack([square_local, inner_local]), "head")
    recip = lax.rsqrt(square_all / width_all + EPS)
    normed = (flat * recip[:, None] * gain).astype(jnp.bfloat16)
    grad_flat = (
        recip[:, None] * upstream - flat * (recip * recip * recip * inner_all / width_all)[:, None]
    )
    grad_out = split_heads(grad_flat.astype(jnp.bfloat16))
    grad_scores = jnp.einsum(
        "thd,shd->hts", grad_out, value_local, preferred_element_type=jnp.float32
    )
    grad_masked = jnp.where(causal[None], grad_scores, 0.0).astype(jnp.bfloat16)
    query_grad = jnp.einsum(
        "hts,shd->thd", grad_masked, key_local, preferred_element_type=jnp.float32
    )
    query_grad = query_grad + jnp.einsum(
        "the,hde->thd", grad_out, carried_bf, preferred_element_type=jnp.float32
    )
    local_grad = jnp.einsum("thd,the->hde", queries, grad_out, preferred_element_type=jnp.float32)
    later = prefix(local_grad, True)
    later_bf = later.astype(jnp.bfloat16)
    key_grad = jnp.einsum("hts,thd->shd", grad_masked, queries, preferred_element_type=jnp.float32)
    key_grad = key_grad + jnp.einsum(
        "she,hde->shd", value_local, later_bf, preferred_element_type=jnp.float32
    )
    value_grad = jnp.einsum("hts,thd->shd", masked, grad_out, preferred_element_type=jnp.float32)
    value_grad = value_grad + jnp.einsum(
        "shd,hde->she", key_local, later_bf, preferred_element_type=jnp.float32
    )
    shape = (tokens_here, heads_here * HEAD_DIM)
    return (
        normed,
        query_grad.reshape(shape).astype(jnp.bfloat16),
        key_grad.reshape(shape).astype(jnp.bfloat16),
        value_grad.reshape(shape).astype(jnp.bfloat16),
    )


def ctx_split(mesh):
    ctx_devices = mesh.devices[:, 0]
    rows_n = len({device.coords[1] for device in ctx_devices})
    cols_n = len(ctx_devices) // rows_n
    return rows_n, 4, cols_n // 4


def solution(mesh):
    heads_n = mesh.devices.shape[1]
    split = Mesh(mesh.devices.reshape(ctx_split(mesh) + (heads_n,)), CTX_AXES + ("head",))
    rows = P(CTX_AXES, "head")
    placed = (rows, rows, rows, P("head"), rows)
    return jax.shard_map(
        on_device,
        mesh=split,
        in_specs=placed,
        out_specs=(rows, rows, rows, rows),
        check_vma=False,
    )
```

```python
import jax
import jax.numpy as jnp
from jax import lax
from jax.sharding import Mesh, PartitionSpec as P

HEADS = 32
HEAD_DIM = 64


EPS = 1e-05


CTX_AXES = ("ctx_rows", "ctx_hi", "ctx_lo")
PEER_AXES = ("ctx_lo", "ctx_rows", "ctx_hi")


def ctx_of_peer(peers):
    sizes = {axis: lax.axis_size(axis) for axis in CTX_AXES}
    slot = lax.broadcasted_iota(jnp.int32, (peers,), 0)
    place = {}
    for axis in reversed(PEER_AXES):
        place[axis] = slot % sizes[axis]
        slot = slot // sizes[axis]
    index = jnp.zeros((peers,), jnp.int32)
    for axis in CTX_AXES:
        index = index * sizes[axis] + place[axis]
    return index


def prefix(value, reverse):
    peers = lax.axis_size(CTX_AXES)
    rows = value.reshape(peers, -1)
    mine = lax.all_to_all(rows, PEER_AXES, 0, 0, tiled=True)
    order = ctx_of_peer(peers)
    row, col = order[:, None], order[None, :]
    before = (col > row) if reverse else (col < row)
    total = jnp.dot(before.astype(mine.dtype), mine, precision=lax.Precision.HIGHEST)
    back = lax.all_to_all(total, PEER_AXES, 0, 0, tiled=True)
    return lax.optimization_barrier(back).reshape(value.shape)


def head_sum(value, axis):
    peers = lax.axis_size(axis)
    spread = jnp.broadcast_to(value[None], (peers,) + value.shape)
    gathered = lax.all_to_all(spread, axis, 0, 0, tiled=True)
    return jnp.sum(gathered, axis=0)


def on_device(query_rows, key_rows, value_rows, norm_gain, cotangent):
    tokens_here = query_rows.shape[0]
    heads_here = query_rows.shape[1] // HEAD_DIM
    width_all = HEADS * HEAD_DIM

    def split_heads(array):
        return array.reshape(tokens_here, heads_here, HEAD_DIM)

    queries = split_heads(query_rows)
    key_local = split_heads(key_rows)
    value_local = split_heads(value_rows)
    gain = norm_gain.astype(jnp.float32)
    causal = lax.broadcasted_iota(jnp.int32, (tokens_here, tokens_here), 0) >= lax.broadcasted_iota(
        jnp.int32, (tokens_here, tokens_here), 1
    )
    local_state = jnp.einsum(
        "thd,the->hde", key_local, value_local, preferred_element_type=jnp.float32
    )
    carried = prefix(local_state, False)
    carried_bf = carried.astype(jnp.bfloat16)
    scores = jnp.einsum("thd,shd->hts", queries, key_local, preferred_element_type=jnp.float32)
    masked = jnp.where(causal[None], scores, 0.0).astype(jnp.bfloat16)
    attended = jnp.einsum("hts,shd->thd", masked, value_local, preferred_element_type=jnp.float32)
    attended = attended + jnp.einsum(
        "thd,hde->the", queries, carried_bf, preferred_element_type=jnp.float32
    )
    flat = attended.reshape(tokens_here, heads_here * HEAD_DIM)
    square_local = jnp.sum(flat * flat, axis=1)
    upstream = cotangent.astype(jnp.float32) * gain
    inner_local = jnp.sum(upstream * flat, axis=1)
    square_all, inner_all = head_sum(jnp.stack([square_local, inner_local]), "head")
    recip = lax.rsqrt(square_all / width_all + EPS)
    normed = (flat * recip[:, None] * gain).astype(jnp.bfloat16)
    grad_flat = (
        recip[:, None] * upstream - flat * (recip * recip * recip * inner_all / width_all)[:, None]
    )
    grad_out = split_heads(grad_flat.astype(jnp.bfloat16))
    grad_scores = jnp.einsum(
        "thd,shd->hts", grad_out, value_local, preferred_element_type=jnp.float32
    )
    grad_masked = jnp.where(causal[None], grad_scores, 0.0).astype(jnp.bfloat16)
    query_grad = jnp.einsum(
        "hts,shd->thd", grad_masked, key_local, preferred_element_type=jnp.float32
    )
    query_grad = query_grad + jnp.einsum(
        "the,hde->thd", grad_out, carried_bf, preferred_element_type=jnp.float32
    )
    local_grad = jnp.einsum("thd,the->hde", queries, grad_out, preferred_element_type=jnp.float32)
    later = prefix(local_grad, True)
    later_bf = later.astype(jnp.bfloat16)
    key_grad = jnp.einsum("hts,thd->shd", grad_masked, queries, preferred_element_type=jnp.float32)
    key_grad = key_grad + jnp.einsum(
        "she,hde->shd", value_local, later_bf, preferred_element_type=jnp.float32
    )
    value_grad = jnp.einsum("hts,thd->shd", masked, grad_out, preferred_element_type=jnp.float32)
    value_grad = value_grad + jnp.einsum(
        "shd,hde->she", key_local, later_bf, preferred_element_type=jnp.float32
    )
    shape = (tokens_here, heads_here * HEAD_DIM)
    return (
        normed,
        query_grad.reshape(shape).astype(jnp.bfloat16),
        key_grad.reshape(shape).astype(jnp.bfloat16),
        value_grad.reshape(shape).astype(jnp.bfloat16),
    )


def ctx_split(mesh):
    ctx_devices = mesh.devices[:, 0]
    rows_n = len({device.coords[1] for device in ctx_devices})
    cols_n = len(ctx_devices) // rows_n
    return rows_n, 2, cols_n // 2


def solution(mesh):
    heads_n = mesh.devices.shape[1]
    split = Mesh(mesh.devices.reshape(ctx_split(mesh) + (heads_n,)), CTX_AXES + ("head",))
    rows = P(CTX_AXES, "head")
    placed = (rows, rows, rows, P("head"), rows)
    return jax.shard_map(
        on_device,
        mesh=split,
        in_specs=placed,
        out_specs=(rows, rows, rows, rows),
        check_vma=False,
    )
```
